256 devices in a mesh: grp: 8 (over y_hi, x), dom: 32 (over y_lo, z, core).
Axes of the slice: x: 4, y: 4 (y_hi: 2, y_lo: 2; y = y_hi * 2 + y_lo), z: 8, core: 2. Of those that a mesh axis runs over, the one named last changes fastest.
Arguments:
- fine_matrix_blocks: bfloat16 [16384, 64, 768], P(('grp', 'dom')), may hold values from -0.21875 to 0.21875
- prolongator: bfloat16 [16384, 64, 64], P(('grp', 'dom')), may hold values from -1.5 to 1.5
- block_columns: int32 [16384, 12], P(('grp', 'dom')), may hold values from 0 to 16383, as said below
- block_aggregates: int32 [16384, 12], P(('grp', 'dom')), may hold values from 0 to 1023, as said below
- live_counts: int32 [256], P(('grp', 'dom')), may hold values from 16 to 64, as said below
Outputs:
- coarse_operator: float32 [1024, 64, 768], P('dom')
The draws below stay inside these ranges and needn't reach their ends.
Inputs may be any that keep to these rules, and one draw needn't show every extreme that they name: live_counts[p] counts the first slots of partition p that hold block rows; some partition has 64 and some has 16. `block_columns`: entry 0 of row i is i itself. For a live row of partition p, every entry is a live row of partition p - 1, p or p + 1 (only partitions that exist); entries may repeat, and repeated blocks add. block_aggregates[i, k] is the aggregate of row block_columns[i, k]. Every row of partition p, with g = p // 32 and q = p % 32, has an aggregate from (((q + 4 * g) % 32) * 8 + g) * 4 to that number plus 4 - 1.
All inputs are finite; a program needn't handle non-finite values.
Results may differ from the reference program's by a relative error of at most 0.0029.
Values may be sent and summed in bfloat16 or wider, within the bound.
No kernel may reach another device: no remote copies, remote signals or barrier semaphores. Data moves between devices by JAX's collectives and lax.ppermute only.
A program may use at most 192 MiB of HBM per device.

```python
import jax
import jax.numpy as jnp
from jax import lax

BLOCK_ORDER = 64
ROW_BLOCK_COUNT = 12
CAP = 64
AGG_DEV = 4
GROUP_COUNT = 8
GROUP_PARTS = 32
GROUP_STRIDE = 4
SLOT_COUNT = 16384
COARSE = 1024


def layout(key):
    partitions = GROUP_COUNT * GROUP_PARTS
    slot_total = CAP * partitions
    subkeys = jax.random.split(jax.random.fold_in(key, 7), 5)
    counts = jax.random.randint(subkeys[0], (partitions,), CAP // 4, CAP + 1)
    busiest = jax.random.randint(subkeys[1], (), 0, partitions)
    positions = jnp.arange(partitions)
    counts = jnp.where(positions == busiest, CAP, counts)
    counts = jnp.where(positions == (busiest + 1) % partitions, CAP // 4, counts)
    own_part = jnp.arange(slot_total) // CAP
    rolled = jax.random.randint(subkeys[2], (slot_total, ROW_BLOCK_COUNT), 0, 10)
    offsets = jnp.where(rolled < 2, -1, jnp.where(rolled >= 8, 1, 0))
    target = own_part[:, None] + offsets
    target = jnp.where((target < 0) | (target >= partitions), own_part[:, None], target)
    drawn_slots = jax.random.randint(subkeys[3], (slot_total, ROW_BLOCK_COUNT), 0, 1048576)
    columns_drawn = target * CAP + drawn_slots % counts[target]
    columns_drawn = columns_drawn.at[:, 0].set(jnp.arange(slot_total))
    local_agg = jax.random.randint(subkeys[4], (slot_total,), 0, AGG_DEV)
    group_index = own_part // GROUP_PARTS
    place_index = own_part % GROUP_PARTS
    first_id = ((place_index + GROUP_STRIDE * group_index) % GROUP_PARTS * GROUP_COUNT + group_index) * AGG_DEV
    row_agg = first_id + local_agg
    return (counts.astype(jnp.int32), columns_drawn.astype(jnp.int32), row_agg[columns_drawn].astype(jnp.int32))


def draw_live_counts(key, part):
    return layout(key)[0]


def draw_block_columns(key, part):
    return layout(key)[1]


def draw_block_aggregates(key, part):
    return layout(key)[2]


def block_levels(own_key, extent, cuts, low, high):
    gain, own = 1.0, jax.random.fold_in(own_key, 6)
    for dim, shards_of in cuts:
        heights = jnp.exp(jax.random.uniform(jax.random.fold_in(own, dim), (shards_of,), jnp.float32, low / len(cuts), high / len(cuts)))
        gain = gain * jnp.repeat(heights, extent[dim] // shards_of).reshape([-1 if axis == dim else 1 for axis in range(len(extent))])
    return gain


def centred(key, shape, width, limit, shards=(), kind=jnp.bfloat16):
    array = jax.random.normal(key, shape, jnp.float32) * width
    if len(shards) > 0:
        array = block_levels(key, shape, shards, -0.22, 0.18) * array
    return jnp.clip(array, min=-limit, max=limit).astype(kind)


def setup_inputs(seed: int = 0) -> dict:
    keys = jax.random.split(jax.random.key(seed), 6)
    return {
        "fine_matrix_blocks": centred(keys[0], (SLOT_COUNT, BLOCK_ORDER, ROW_BLOCK_COUNT * BLOCK_ORDER), (ROW_BLOCK_COUNT * BLOCK_ORDER) ** -0.5, 0.21875, ((0, 256),)),
        "prolongator": centred(keys[1], (SLOT_COUNT, BLOCK_ORDER, BLOCK_ORDER), 16 ** -0.5, 1.5, ((0, 256),)),
        "block_columns": draw_block_columns(jax.random.fold_in(keys[5], 71), 0),
        "block_aggregates": draw_block_aggregates(jax.random.fold_in(keys[5], 71), 0),
        "live_counts": draw_live_counts(jax.random.fold_in(keys[5], 71), 0),
    }


def reference(fine_matrix_blocks, prolongator, block_columns, block_aggregates, live_counts):
    partitions = GROUP_COUNT * GROUP_PARTS
    slot_width = 3 * AGG_DEV
    matrix_view = fine_matrix_blocks.reshape(SLOT_COUNT, BLOCK_ORDER, ROW_BLOCK_COUNT, BLOCK_ORDER)

    def one_partition(partition):
        start = (partition * CAP).astype(jnp.int32)
        block_rows = lax.dynamic_slice_in_dim(matrix_view, start, CAP, 0).astype(jnp.float32)
        columns = lax.dynamic_slice_in_dim(block_columns, start, CAP, 0)
        aggregates = lax.dynamic_slice_in_dim(block_aggregates, start, CAP, 0)
        own_blocks = lax.dynamic_slice_in_dim(prolongator, start, CAP, 0).astype(jnp.float32)
        gathered = prolongator[columns].astype(jnp.float32)
        products = jnp.einsum("ixky,ikyz->ixkz", block_rows, gathered, precision=lax.Precision.HIGHEST)
        coarse_slot = AGG_DEV * (columns // CAP - partition + 1) + aggregates % AGG_DEV
        live_rows = (jnp.arange(CAP) < live_counts[partition]).astype(jnp.float32)
        slot_select = (coarse_slot[:, :, None] == jnp.arange(slot_width)[None, None, :]).astype(jnp.float32)
        slot_select = slot_select * live_rows[:, None, None]
        row_sums = jnp.einsum("ikt,ixkz->ixtz", slot_select, products, precision=lax.Precision.HIGHEST)
        row_sums = row_sums.astype(jnp.bfloat16).astype(jnp.float32).reshape(CAP * BLOCK_ORDER, slot_width * BLOCK_ORDER)
        row_select = (aggregates[:, 0:1] % AGG_DEV == jnp.arange(AGG_DEV)[None, :]).astype(jnp.float32)
        row_select = row_select * live_rows[:, None]
        spread = (row_select[:, None, :, None] * own_blocks[:, :, None, :]).reshape(CAP * BLOCK_ORDER, AGG_DEV * BLOCK_ORDER)
        coarse = jnp.dot(spread.T, row_sums, precision=lax.Precision.HIGHEST, preferred_element_type=jnp.float32)
        first_block = aggregates[0, 0] // AGG_DEV
        return coarse.reshape(AGG_DEV, BLOCK_ORDER, slot_width * BLOCK_ORDER), first_block

    coarse_all, first_blocks = lax.map(one_partition, jnp.arange(partitions, dtype=jnp.int32))
    positions = (first_blocks[:, None] * AGG_DEV + jnp.arange(AGG_DEV, dtype=jnp.int32)[None, :]).reshape(-1)
    assembled = jnp.zeros((COARSE, BLOCK_ORDER, slot_width * BLOCK_ORDER), jnp.float32)
    assembled = assembled.at[positions].set(coarse_all.reshape(partitions * AGG_DEV, BLOCK_ORDER, slot_width * BLOCK_ORDER))
    return assembled
```

```python
import jax
import jax.numpy as jnp
from jax import lax
from jax.sharding import PartitionSpec as P

AGG_DEV = 4


def extended(block, sides, width):
    for axis, dim in sides:
        count = lax.axis_size(axis)
        forward = [(i, i + 1) for i in range(count - 1)]
        backward = [(target, source) for source, target in forward]
        low = lax.ppermute(
            lax.slice_in_dim(block, block.shape[dim] - width, None, axis=dim), axis, forward
        )
        high = lax.ppermute(lax.slice_in_dim(block, 0, width, axis=dim), axis, backward)
        block = jnp.concatenate([low, block, high], axis=dim)
    return block


def local(fine_matrix_blocks, prolongator, block_columns, block_aggregates, live_counts):
    capacity = fine_matrix_blocks.shape[0]
    block_width = prolongator.shape[1]
    row_blocks = block_columns.shape[1]
    slot_width = 3 * AGG_DEV
    position = lax.axis_index(("grp", "dom"))
    ghosts = extended(prolongator, ((("grp", "dom"), 0),), capacity)
    local_rows = block_columns - (position - 1) * capacity
    gathered = jnp.take(ghosts, local_rows, axis=0)
    matrix_view = fine_matrix_blocks.reshape(capacity, block_width, row_blocks, block_width)
    products = jnp.einsum(
        "ixky,ikyz->ixkz", matrix_view, gathered, preferred_element_type=jnp.float32
    )
    coarse_slot = AGG_DEV * (local_rows // capacity) + block_aggregates % AGG_DEV
    live_rows = jnp.arange(capacity) < live_counts[0]
    slot_select = (coarse_slot[:, :, None] == jnp.arange(slot_width)[None, None, :]) & live_rows[
        :, None, None
    ]
    row_sums = jnp.einsum(
        "ikt,ixkz->ixtz", slot_select.astype(jnp.float32), products, precision=lax.Precision.HIGHEST
    )
    row_sums = row_sums.astype(jnp.bfloat16).reshape(
        capacity * block_width, slot_width * block_width
    )
    row_select = (block_aggregates[:, 0:1] % AGG_DEV == jnp.arange(AGG_DEV)[None, :]) & live_rows[
        :, None
    ]
    spread = row_select.astype(jnp.bfloat16)[:, None, :, None] * prolongator[:, :, None, :]
    spread = spread.reshape(capacity * block_width, AGG_DEV * block_width)
    coarse = lax.dot_general(
        spread, row_sums, (((0,), (0,)), ((), ())), preferred_element_type=jnp.float32
    )
    groups_count = lax.axis_size("grp")
    places = lax.axis_size("dom")
    step_stride = places // groups_count
    pairs = [
        (g * places + q, g * places + (q + step_stride * g) % places)
        for g in range(groups_count)
        for q in range(places)
    ]
    rotated = lax.ppermute(coarse.astype(jnp.bfloat16), ("grp", "dom"), pairs)
    result = lax.all_gather(rotated[None], "grp", axis=0, tiled=True)
    result = result.astype(jnp.float32)
    return result.reshape(groups_count * AGG_DEV, block_width, slot_width * block_width)


def solution(mesh):
    return jax.shard_map(
        local,
        mesh=mesh,
        in_specs=(
            P(("grp", "dom"), None, None),
            P(("grp", "dom"), None, None),
            P(("grp", "dom"), None),
            P(("grp", "dom"), None),
            P(("grp", "dom")),
        ),
        out_specs=P("dom", None, None),
        check_vma=False,
    )
```

```python
import jax
import jax.numpy as jnp
from jax import lax
from jax.experimental import pallas as pl
from jax.experimental.pallas import tpu as pltpu
from jax.sharding import PartitionSpec as P

AGG_DEV = 4


def coarse_kernel(cols_ref, slots_ref, aggs_ref, live_ref, f_ref, wl_ref, wr_ref, pt_ref, o_ref, even_ref, odd_ref):
    step = pl.program_id(0)
    rows = f_ref.shape[0]
    width = pt_ref.shape[1]
    pairs = f_ref.shape[2] // (2 * width)
    slots = even_ref.shape[0]

    @pl.when(step == 0)
    def _():
        o_ref[...] = jnp.zeros_like(o_ref)

    lane = lax.broadcasted_iota(jnp.int32, (width, 2 * width), 1)
    low_half = lane < width

    def row(r, carry):
        i = step * rows + r
        even_ref[...] = jnp.zeros_like(even_ref)
        odd_ref[...] = jnp.zeros_like(odd_ref)
        for j in range(pairs):
            first = i * (2 * pairs) + 2 * j
            block = jnp.concatenate([wl_ref[cols_ref[first]], wr_ref[cols_ref[first + 1]]], axis=0)
            part = jnp.dot(
                f_ref[r, :, 2 * width * j : 2 * width * (j + 1)], block, preferred_element_type=jnp.float32
            )
            t_even = slots_ref[first]
            t_odd = slots_ref[first + 1]
            even_ref[t_even] += part
            odd_ref[t_odd] += part
        live = i < live_ref[0]
        tiles = []
        for u in range(slots // 2):
            left = even_ref[2 * u] + pltpu.roll(odd_ref[2 * u], width, 1)
            right = pltpu.roll(even_ref[2 * u + 1], width, 1) + odd_ref[2 * u + 1]
            tiles.append(jnp.where(low_half, left, right))
        sums = jnp.concatenate(tiles, axis=1)
        sums = jnp.where(live, sums, 0.0).astype(jnp.bfloat16).astype(pt_ref.dtype)
        a = aggs_ref[i]
        o_ref[a] += jnp.dot(pt_ref[r], sums, preferred_element_type=jnp.float32)
        return carry

    lax.fori_loop(0, rows, row, 0)


def coarse_rows(fine, ghosts, local_rows, slots, aggs, live_count, rows=8, interpret=False):
    capacity, width, span = fine.shape
    slot_width = 3 * AGG_DEV
    ghost_count = ghosts.shape[0]
    wl = jnp.pad(ghosts, ((0, 0), (0, 0), (0, width)))
    wr = jnp.pad(ghosts, ((0, 0), (0, 0), (width, 0)))
    transposed = jnp.swapaxes(ghosts[capacity : 2 * capacity], 1, 2)
    grid_spec = pltpu.PrefetchScalarGridSpec(
        num_scalar_prefetch=4,
        grid=(capacity // rows,),
        in_specs=[
            pl.BlockSpec((rows, width, span), lambda b, *_: (b, 0, 0)),
            pl.BlockSpec((ghost_count, width, 2 * width), lambda b, *_: (0, 0, 0)),
            pl.BlockSpec((ghost_count, width, 2 * width), lambda b, *_: (0, 0, 0)),
            pl.BlockSpec((rows, width, width), lambda b, *_: (b, 0, 0)),
        ],
        out_specs=pl.BlockSpec((AGG_DEV, width, slot_width * width), lambda b, *_: (0, 0, 0)),
        scratch_shapes=[
            pltpu.VMEM((slot_width, width, 2 * width), jnp.float32),
            pltpu.VMEM((slot_width, width, 2 * width), jnp.float32),
        ],
    )
    return pl.pallas_call(
        coarse_kernel,
        grid_spec=grid_spec,
        out_shape=jax.ShapeDtypeStruct((AGG_DEV, width, slot_width * width), jnp.float32),
        compiler_params=pltpu.CompilerParams(dimension_semantics=("arbitrary",)),
        interpret=interpret,
    )(local_rows.reshape(-1), slots.reshape(-1), aggs, live_count, fine, wl, wr, transposed)


def extended(block, sides, width):
    for axis, dim in sides:
        count = lax.axis_size(axis)
        forward = [(i, i + 1) for i in range(count - 1)]
        backward = [(target, source) for source, target in forward]
        low = lax.ppermute(
            lax.slice_in_dim(block, block.shape[dim] - width, None, axis=dim), axis, forward
        )
        high = lax.ppermute(lax.slice_in_dim(block, 0, width, axis=dim), axis, backward)
        block = jnp.concatenate([low, block, high], axis=dim)
    return block


def local(fine_matrix_blocks, prolongator, block_columns, block_aggregates, live_counts):
    capacity = fine_matrix_blocks.shape[0]
    position = lax.axis_index(("grp", "dom"))
    ghosts = extended(prolongator, ((("grp", "dom"), 0),), capacity)
    local_rows = jnp.clip(block_columns - (position - 1) * capacity, 0, 3 * capacity - 1)
    slots = jnp.clip(AGG_DEV * (local_rows // capacity) + block_aggregates % AGG_DEV, 0, 3 * AGG_DEV - 1)
    aggs = block_aggregates[:, 0] % AGG_DEV
    coarse = coarse_rows(fine_matrix_blocks, ghosts, local_rows, slots, aggs, live_counts)
    groups_count = lax.axis_size("grp")
    places = lax.axis_size("dom")
    step_stride = places // groups_count
    pairs = [
        (g * places + q, g * places + (q + step_stride * g) % places)
        for g in range(groups_count)
        for q in range(places)
    ]
    rotated = lax.ppermute(coarse.astype(jnp.bfloat16), ("grp", "dom"), pairs)
    copies = jnp.broadcast_to(rotated[None], (groups_count,) + rotated.shape)
    result = lax.all_to_all(copies, "grp", 0, 0, tiled=True).astype(jnp.float32)
    return result.reshape((groups_count * AGG_DEV,) + coarse.shape[1:])


def solution(mesh):
    return jax.shard_map(
        local,
        mesh=mesh,
        in_specs=(
            P(("grp", "dom"), None, None),
            P(("grp", "dom"), None, None),
            P(("grp", "dom"), None),
            P(("grp", "dom"), None),
            P(("grp", "dom")),
        ),
        out_specs=P("dom", None, None),
        check_vma=False,
    )
```

```python
import functools
import jax
import jax.numpy as jnp
from jax import lax
from jax.experimental import pallas as pl
from jax.experimental.pallas import tpu as pltpu
from jax.sharding import PartitionSpec as P

AGG_DEV = 4


def coarse_kernel(cols_ref, aggs_ref, live_ref, base_ref, f_ref, g_ref, p_ref, o_ref, even_ref, odd_ref, *, group, transpose_lhs, capacity):
    step = pl.program_id(0)
    rows = f_ref.shape[0]
    width = p_ref.shape[1]
    blocks = f_ref.shape[2] // width
    slots = even_ref.shape[0]
    ghost_count = g_ref.shape[0]

    @pl.when(step == 0)
    def _():
        o_ref[...] = jnp.zeros_like(o_ref)

    lane = lax.broadcasted_iota(jnp.int32, (width, 2 * width), 1)
    low_half = lane < width
    base = base_ref[0]

    def place(r_i, k):
        c = jnp.clip(cols_ref[r_i, k] - base, 0, ghost_count - 1)
        t = AGG_DEV * (c // capacity) + jnp.bitwise_and(aggs_ref[r_i, k], AGG_DEV - 1)
        return c, t

    def row(r, carry):
        i = step * rows + r
        even_ref[...] = jnp.zeros_like(even_ref)
        odd_ref[...] = jnp.zeros_like(odd_ref)
        for j in range(blocks // group):
            ks = [group * j + m for m in range(group)]
            placed = [place(i, k) for k in ks]
            pieces = []
            for m, (c, _) in enumerate(placed):
                tile = g_ref[c]
                pieces.append(jnp.where(low_half if m % 2 == 0 else ~low_half, tile, jnp.zeros_like(tile)))
            if group == 2:
                block = jnp.concatenate(pieces, axis=0)
            else:
                zero = jnp.zeros((2 * width, 2 * width), pieces[0].dtype)
                top = jnp.concatenate([jnp.concatenate(pieces[:2], axis=0), zero], axis=1)
                bottom = jnp.concatenate([zero, jnp.concatenate(pieces[2:], axis=0)], axis=1)
                block = jnp.concatenate([top, bottom], axis=0)
            part = jnp.dot(
                f_ref[r, :, group * width * j : group * width * (j + 1)], block, preferred_element_type=jnp.float32
            )
            for h in range(group // 2):
                half = part[:, 2 * width * h : 2 * width * (h + 1)]
                even_ref[placed[2 * h][1]] += half
                odd_ref[placed[2 * h + 1][1]] += half
        live = i < live_ref[0]
        tiles = []
        for u in range(slots // 2):
            left = even_ref[2 * u] + pltpu.roll(odd_ref[2 * u], width, 1)
            right = pltpu.roll(even_ref[2 * u + 1], width, 1) + odd_ref[2 * u + 1]
            tiles.append(jnp.where(low_half, left, right))
        sums = jnp.concatenate(tiles, axis=1)
        sums = jnp.where(live, sums, 0.0).astype(jnp.bfloat16).astype(p_ref.dtype)
        a = jnp.bitwise_and(aggs_ref[i, 0], AGG_DEV - 1)
        if transpose_lhs:
            contrib = lax.dot_general(p_ref[r], sums, (((0,), (0,)), ((), ())), preferred_element_type=jnp.float32)
        else:
            contrib = jnp.dot(p_ref[r].T, sums, preferred_element_type=jnp.float32)
        o_ref[a] += contrib
        return carry

    lax.fori_loop(0, rows, row, 0)


def coarse_rows(fine, ghosts, own, cols, aggs, live_count, base, rows=8, group=2, transpose_lhs=True, interpret=False):
    capacity, width, span = fine.shape
    slot_width = 3 * AGG_DEV
    ghost_count = ghosts.shape[0]
    doubled = jnp.concatenate([ghosts, ghosts], axis=2)
    grid_spec = pltpu.PrefetchScalarGridSpec(
        num_scalar_prefetch=4,
        grid=(capacity // rows,),
        in_specs=[
            pl.BlockSpec((rows, width, span), lambda b, *_: (b, 0, 0)),
            pl.BlockSpec((ghost_count, width, 2 * width), lambda b, *_: (0, 0, 0)),
            pl.BlockSpec((rows, width, width), lambda b, *_: (b, 0, 0)),
        ],
        out_specs=pl.BlockSpec((AGG_DEV, width, slot_width * width), lambda b, *_: (0, 0, 0)),
        scratch_shapes=[
            pltpu.VMEM((slot_width, width, 2 * width), jnp.float32),
            pltpu.VMEM((slot_width, width, 2 * width), jnp.float32),
        ],
    )
    kernel = functools.partial(coarse_kernel, group=group, transpose_lhs=transpose_lhs, capacity=capacity)
    return pl.pallas_call(
        kernel,
        grid_spec=grid_spec,
        out_shape=jax.ShapeDtypeStruct((AGG_DEV, width, slot_width * width), jnp.float32),
        compiler_params=pltpu.CompilerParams(dimension_semantics=("arbitrary",)),
        interpret=interpret,
    )(cols, aggs, live_count, base, fine, doubled, own)


def extended(block, sides, width):
    for axis, dim in sides:
        count = lax.axis_size(axis)
        forward = [(i, i + 1) for i in range(count - 1)]
        backward = [(target, source) for source, target in forward]
        low = lax.ppermute(
            lax.slice_in_dim(block, block.shape[dim] - width, None, axis=dim), axis, forward
        )
        high = lax.ppermute(lax.slice_in_dim(block, 0, width, axis=dim), axis, backward)
        block = jnp.concatenate([low, block, high], axis=dim)
    return block


def local(fine_matrix_blocks, prolongator, block_columns, block_aggregates, live_counts):
    capacity = fine_matrix_blocks.shape[0]
    position = lax.axis_index(("grp", "dom"))
    ghosts = extended(prolongator, ((("grp", "dom"), 0),), capacity)
    base = jnp.reshape((position - 1) * capacity, (1,)).astype(jnp.int32)
    coarse = coarse_rows(
        fine_matrix_blocks, ghosts, prolongator, block_columns, block_aggregates, live_counts, base
    )
    groups_count = lax.axis_size("grp")
    places = lax.axis_size("dom")
    step_stride = places // groups_count
    pairs = [
        (g * places + q, g * places + (q + step_stride * g) % places)
        for g in range(groups_count)
        for q in range(places)
    ]
    rotated = lax.ppermute(coarse.astype(jnp.bfloat16), ("grp", "dom"), pairs)
    copies = jnp.broadcast_to(rotated[None], (groups_count,) + rotated.shape)
    result = lax.all_to_all(copies, "grp", 0, 0, tiled=True).astype(jnp.float32)
    return result.reshape((groups_count * AGG_DEV,) + coarse.shape[1:])


def solution(mesh):
    return jax.shard_map(
        local,
        mesh=mesh,
        in_specs=(
            P(("grp", "dom"), None, None),
            P(("grp", "dom"), None, None),
            P(("grp", "dom"), None),
            P(("grp", "dom"), None),
            P(("grp", "dom")),
        ),
        out_specs=P("dom", None, None),
        check_vma=False,
    )
```

```python
import functools
import jax
import jax.numpy as jnp
from jax import lax
from jax.experimental import pallas as pl
from jax.experimental.pallas import tpu as pltpu
from jax.sharding import PartitionSpec as P

AGG_DEV = 4


def coarse_kernel(
    cols_ref, aggs_ref, live_ref, base_ref, f_ref, g_ref, p_ref, o_ref, even_ref, odd_ref, *, group, transpose_lhs, capacity, half
):
    step = pl.program_id(0)
    rows = f_ref.shape[0]
    width = p_ref.shape[1]
    blocks = f_ref.shape[2] // width
    slots = even_ref.shape[0]
    ghost_count = g_ref.shape[0]

    @pl.when(step == 0)
    def _():
        o_ref[...] = jnp.zeros_like(o_ref)

    lane = lax.broadcasted_iota(jnp.int32, (width, 2 * width), 1)
    low_half = lane < width
    base = base_ref[0]

    def place(r_i, k):
        c = jnp.clip(cols_ref[r_i, k] - base, 0, ghost_count - 1)
        t = AGG_DEV * (c // capacity) + jnp.bitwise_and(aggs_ref[r_i, k], AGG_DEV - 1)
        return c, t

    def row(r, carry):
        i = step * rows + r
        a = jnp.bitwise_and(aggs_ref[i, 0], AGG_DEV - 1)
        kept = o_ref.shape[0]

        @pl.when(a // kept == half)
        def _():
            one_row(r, i, a - kept * half)

        return carry

    def one_row(r, i, a):
        even_ref[...] = jnp.zeros_like(even_ref)
        odd_ref[...] = jnp.zeros_like(odd_ref)
        for j in range(blocks // group):
            ks = [group * j + m for m in range(group)]
            placed = [place(i, k) for k in ks]
            pieces = []
            for m, (c, _) in enumerate(placed):
                tile = g_ref[c]
                pieces.append(jnp.where(low_half if m % 2 == 0 else ~low_half, tile, jnp.zeros_like(tile)))
            if group == 2:
                block = jnp.concatenate(pieces, axis=0)
            else:
                zero = jnp.zeros((2 * width, 2 * width), pieces[0].dtype)
                top = jnp.concatenate([jnp.concatenate(pieces[:2], axis=0), zero], axis=1)
                bottom = jnp.concatenate([zero, jnp.concatenate(pieces[2:], axis=0)], axis=1)
                block = jnp.concatenate([top, bottom], axis=0)
            part = jnp.dot(
                f_ref[r, :, group * width * j : group * width * (j + 1)], block, preferred_element_type=jnp.float32
            )
            for h in range(group // 2):
                piece = part[:, 2 * width * h : 2 * width * (h + 1)]
                even_ref[placed[2 * h][1]] += piece
                odd_ref[placed[2 * h + 1][1]] += piece
        live = i < live_ref[0]
        tiles = []
        for u in range(slots // 2):
            left = even_ref[2 * u] + pltpu.roll(odd_ref[2 * u], width, 1)
            right = pltpu.roll(even_ref[2 * u + 1], width, 1) + odd_ref[2 * u + 1]
            tiles.append(jnp.where(low_half, left, right))
        sums = jnp.concatenate(tiles, axis=1)
        sums = jnp.where(live, sums, 0.0).astype(jnp.bfloat16).astype(p_ref.dtype)
        if transpose_lhs:
            contrib = lax.dot_general(p_ref[r], sums, (((0,), (0,)), ((), ())), preferred_element_type=jnp.float32)
        else:
            contrib = jnp.dot(p_ref[r].T, sums, preferred_element_type=jnp.float32)
        o_ref[a] += contrib

    lax.fori_loop(0, rows, row, 0)


def coarse_rows(
    fine, ghosts, own, cols, aggs, live_count, base, half, kept, rows=8, group=2, transpose_lhs=True, interpret=False
):
    capacity, width, span = fine.shape
    slot_width = 3 * AGG_DEV
    ghost_count = ghosts.shape[0]
    doubled = ghosts
    grid_spec = pltpu.PrefetchScalarGridSpec(
        num_scalar_prefetch=4,
        grid=(capacity // rows,),
        in_specs=[
            pl.BlockSpec((rows, width, span), lambda b, *_: (b, 0, 0)),
            pl.BlockSpec(ghosts.shape, lambda b, *_: (0, 0, 0)),
            pl.BlockSpec((rows, width, width), lambda b, *_: (b, 0, 0)),
        ],
        out_specs=pl.BlockSpec((kept, width, slot_width * width), lambda b, *_: (0, 0, 0)),
        scratch_shapes=[
            pltpu.VMEM((slot_width, width, 2 * width), jnp.float32),
            pltpu.VMEM((slot_width, width, 2 * width), jnp.float32),
        ],
    )
    kernel = functools.partial(
        coarse_kernel, group=group, transpose_lhs=transpose_lhs, capacity=capacity, half=half
    )
    return pl.pallas_call(
        kernel,
        grid_spec=grid_spec,
        out_shape=jax.ShapeDtypeStruct((kept, width, slot_width * width), jnp.float32),
        compiler_params=pltpu.CompilerParams(dimension_semantics=("arbitrary",)),
        interpret=interpret,
    )(cols, aggs, live_count, base, fine, doubled, own)


def extended(block, sides, width):
    for axis, dim in sides:
        count = lax.axis_size(axis)
        forward = [(i, i + 1) for i in range(count - 1)]
        backward = [(target, source) for source, target in forward]
        low = lax.ppermute(
            lax.slice_in_dim(block, block.shape[dim] - width, None, axis=dim), axis, forward
        )
        high = lax.ppermute(lax.slice_in_dim(block, 0, width, axis=dim), axis, backward)
        block = jnp.concatenate([low, block, high], axis=dim)
    return block


def local(fine_matrix_blocks, prolongator, block_columns, block_aggregates, live_counts):
    capacity = fine_matrix_blocks.shape[0]
    position = lax.axis_index(("grp", "dom"))
    ghosts = extended(prolongator, ((("grp", "dom"), 0),), capacity)
    base = jnp.reshape((position - 1) * capacity, (1,)).astype(jnp.int32)
    doubled = jnp.concatenate([ghosts, ghosts], axis=2)
    groups_count = lax.axis_size("grp")
    places = lax.axis_size("dom")
    step_stride = places // groups_count
    pairs = [
        (g * places + q, g * places + (q + step_stride * g) % places)
        for g in range(groups_count)
        for q in range(places)
    ]
    halves = 2
    kept = AGG_DEV // halves
    gathered = []
    for half in range(halves):
        coarse = coarse_rows(
            fine_matrix_blocks, doubled, prolongator, block_columns, block_aggregates, live_counts, base, half, kept
        )
        rotated = lax.ppermute(coarse.astype(jnp.bfloat16), ("grp", "dom"), pairs)
        copies = jnp.broadcast_to(rotated[None], (groups_count,) + rotated.shape)
        gathered.append(lax.all_to_all(copies, "grp", 0, 0, tiled=True))
    result = jnp.concatenate(gathered, axis=1).astype(jnp.float32)
    return result.reshape((groups_count * AGG_DEV,) + coarse.shape[1:])


def solution(mesh):
    return jax.shard_map(
        local,
        mesh=mesh,
        in_specs=(
            P(("grp", "dom"), None, None),
            P(("grp", "dom"), None, None),
            P(("grp", "dom"), None),
            P(("grp", "dom"), None),
            P(("grp", "dom")),
        ),
        out_specs=P("dom", None, None),
        check_vma=False,
    )
```

```python
import functools
import jax
import jax.numpy as jnp
from jax import lax
from jax.experimental import pallas as pl
from jax.experimental.pallas import tpu as pltpu
from jax.sharding import PartitionSpec as P

AGG_DEV = 4


def coarse_kernel(cols_ref, aggs_ref, live_ref, base_ref, f_ref, g_ref, p_ref, o_ref, even_ref, odd_ref, *, group, transpose_lhs, capacity):
    step = pl.program_id(0)
    rows = f_ref.shape[0]
    width = p_ref.shape[1]
    blocks = f_ref.shape[2] // width
    slots = even_ref.shape[0]
    ghost_count = g_ref.shape[0]

    @pl.when(step == 0)
    def _():
        o_ref[...] = jnp.zeros_like(o_ref)

    lane = lax.broadcasted_iota(jnp.int32, (width, 2 * width), 1)
    low_half = lane < width
    base = base_ref[0]

    def place(r_i, k):
        c = jnp.clip(cols_ref[r_i, k] - base, 0, ghost_count - 1)
        t = AGG_DEV * (c // capacity) + jnp.bitwise_and(aggs_ref[r_i, k], AGG_DEV - 1)
        return c, t

    def row(r, carry):
        i = step * rows + r
        even_ref[...] = jnp.zeros_like(even_ref)
        odd_ref[...] = jnp.zeros_like(odd_ref)
        for j in range(blocks // group):
            ks = [group * j + m for m in range(group)]
            placed = [place(i, k) for k in ks]
            pieces = []
            for m, (c, _) in enumerate(placed):
                tile = g_ref[c]
                pieces.append(jnp.where(low_half if m % 2 == 0 else ~low_half, tile, jnp.zeros_like(tile)))
            if group == 2:
                block = jnp.concatenate(pieces, axis=0)
            else:
                zero = jnp.zeros((2 * width, 2 * width), pieces[0].dtype)
                top = jnp.concatenate([jnp.concatenate(pieces[:2], axis=0), zero], axis=1)
                bottom = jnp.concatenate([zero, jnp.concatenate(pieces[2:], axis=0)], axis=1)
                block = jnp.concatenate([top, bottom], axis=0)
            part = jnp.dot(
                f_ref[r, :, group * width * j : group * width * (j + 1)], block, preferred_element_type=jnp.float32
            )
            for h in range(group // 2):
                half = part[:, 2 * width * h : 2 * width * (h + 1)]
                even_ref[placed[2 * h][1]] += half
                odd_ref[placed[2 * h + 1][1]] += half
        live = i < live_ref[0]
        tiles = []
        for u in range(slots // 2):
            left = even_ref[2 * u] + pltpu.roll(odd_ref[2 * u], width, 1)
            right = pltpu.roll(even_ref[2 * u + 1], width, 1) + odd_ref[2 * u + 1]
            tiles.append(jnp.where(low_half, left, right))
        sums = jnp.concatenate(tiles, axis=1)
        sums = jnp.where(live, sums, 0.0).astype(jnp.bfloat16).astype(p_ref.dtype)
        a = jnp.bitwise_and(aggs_ref[i, 0], AGG_DEV - 1)
        if transpose_lhs:
            contrib = lax.dot_general(p_ref[r], sums, (((0,), (0,)), ((), ())), preferred_element_type=jnp.float32)
        else:
            contrib = jnp.dot(p_ref[r].T, sums, preferred_element_type=jnp.float32)
        o_ref[a] += contrib
        return carry

    for r in range(rows):
        row(r, 0)


def coarse_rows(fine, ghosts, own, cols, aggs, live_count, base, rows=8, group=2, transpose_lhs=True, interpret=False):
    capacity, width, span = fine.shape
    slot_width = 3 * AGG_DEV
    ghost_count = ghosts.shape[0]
    doubled = jnp.concatenate([ghosts, ghosts], axis=2)
    grid_spec = pltpu.PrefetchScalarGridSpec(
        num_scalar_prefetch=4,
        grid=(capacity // rows,),
        in_specs=[
            pl.BlockSpec((rows, width, span), lambda b, *_: (b, 0, 0)),
            pl.BlockSpec((ghost_count, width, 2 * width), lambda b, *_: (0, 0, 0)),
            pl.BlockSpec((rows, width, width), lambda b, *_: (b, 0, 0)),
        ],
        out_specs=pl.BlockSpec((AGG_DEV, width, slot_width * width), lambda b, *_: (0, 0, 0)),
        scratch_shapes=[
            pltpu.VMEM((slot_width, width, 2 * width), jnp.float32),
            pltpu.VMEM((slot_width, width, 2 * width), jnp.float32),
        ],
    )
    kernel = functools.partial(coarse_kernel, group=group, transpose_lhs=transpose_lhs, capacity=capacity)
    return pl.pallas_call(
        kernel,
        grid_spec=grid_spec,
        out_shape=jax.ShapeDtypeStruct((AGG_DEV, width, slot_width * width), jnp.float32),
        compiler_params=pltpu.CompilerParams(dimension_semantics=("arbitrary",)),
        interpret=interpret,
    )(cols, aggs, live_count, base, fine, doubled, own)


def extended(block, sides, width):
    for axis, dim in sides:
        count = lax.axis_size(axis)
        forward = [(i, i + 1) for i in range(count - 1)]
        backward = [(target, source) for source, target in forward]
        low = lax.ppermute(
            lax.slice_in_dim(block, block.shape[dim] - width, None, axis=dim), axis, forward
        )
        high = lax.ppermute(lax.slice_in_dim(block, 0, width, axis=dim), axis, backward)
        block = jnp.concatenate([low, block, high], axis=dim)
    return block


def local(fine_matrix_blocks, prolongator, block_columns, block_aggregates, live_counts):
    capacity = fine_matrix_blocks.shape[0]
    position = lax.axis_index(("grp", "dom"))
    ghosts = extended(prolongator, ((("grp", "dom"), 0),), capacity)
    base = jnp.reshape((position - 1) * capacity, (1,)).astype(jnp.int32)
    coarse = coarse_rows(
        fine_matrix_blocks, ghosts, prolongator, block_columns, block_aggregates, live_counts, base
    )
    groups_count = lax.axis_size("grp")
    places = lax.axis_size("dom")
    step_stride = places // groups_count
    pairs = [
        (g * places + q, g * places + (q + step_stride * g) % places)
        for g in range(groups_count)
        for q in range(places)
    ]
    rotated = lax.ppermute(coarse.astype(jnp.bfloat16), ("grp", "dom"), pairs)
    copies = jnp.broadcast_to(rotated[None], (groups_count,) + rotated.shape)
    result = lax.all_to_all(copies, "grp", 0, 0, tiled=True).astype(jnp.float32)
    return result.reshape((groups_count * AGG_DEV,) + coarse.shape[1:])


def solution(mesh):
    return jax.shard_map(
        local,
        mesh=mesh,
        in_specs=(
            P(("grp", "dom"), None, None),
            P(("grp", "dom"), None, None),
            P(("grp", "dom"), None),
            P(("grp", "dom"), None),
            P(("grp", "dom")),
        ),
        out_specs=P("dom", None, None),
        check_vma=False,
    )
```

```python
import functools
import jax
import jax.numpy as jnp
from jax import lax
from jax.experimental import pallas as pl
from jax.experimental.pallas import tpu as pltpu
from jax.sharding import PartitionSpec as P

AGG_DEV = 4


def coarse_kernel(cols_ref, aggs_ref, live_ref, base_ref, f_ref, g_ref, p_ref, o_ref, even_ref, odd_ref, s_ref, *, group, transpose_lhs, capacity):
    step = pl.program_id(0)
    rows = f_ref.shape[0]
    width = p_ref.shape[1]
    blocks = f_ref.shape[2] // width
    slots = even_ref.shape[0]
    ghost_count = g_ref.shape[0]

    @pl.when(step == 0)
    def _():
        o_ref[...] = jnp.zeros_like(o_ref)

    lane = lax.broadcasted_iota(jnp.int32, (width, 2 * width), 1)
    low_half = lane < width
    base = base_ref[0]

    def place(r_i, k):
        c = jnp.clip(cols_ref[k, r_i] - base, 0, ghost_count - 1)
        t = AGG_DEV * (c // capacity) + jnp.bitwise_and(aggs_ref[k, r_i], AGG_DEV - 1)
        return c, t

    def row(r, carry):
        i = step * rows + r
        even_ref[...] = jnp.zeros_like(even_ref)
        odd_ref[...] = jnp.zeros_like(odd_ref)
        for j in range(blocks // group):
            ks = [group * j + m for m in range(group)]
            placed = [place(i, k) for k in ks]
            pieces = []
            for m, (c, _) in enumerate(placed):
                tile = g_ref[c]
                pieces.append(jnp.where(low_half if m % 2 == 0 else ~low_half, tile, jnp.zeros_like(tile)))
            if group == 2:
                block = jnp.concatenate(pieces, axis=0)
            else:
                zero = jnp.zeros((2 * width, 2 * width), pieces[0].dtype)
                top = jnp.concatenate([jnp.concatenate(pieces[:2], axis=0), zero], axis=1)
                bottom = jnp.concatenate([zero, jnp.concatenate(pieces[2:], axis=0)], axis=1)
                block = jnp.concatenate([top, bottom], axis=0)
            part = jnp.dot(
                f_ref[r, :, group * width * j : group * width * (j + 1)], block, preferred_element_type=jnp.float32
            )
            for h in range(group // 2):
                half = part[:, 2 * width * h : 2 * width * (h + 1)]
                even_ref[placed[2 * h][1]] += half
                odd_ref[placed[2 * h + 1][1]] += half
        live = i < live_ref[0]
        tiles = []
        for u in range(slots // 2):
            left = even_ref[2 * u] + pltpu.roll(odd_ref[2 * u], width, 1)
            right = pltpu.roll(even_ref[2 * u + 1], width, 1) + odd_ref[2 * u + 1]
            tiles.append(jnp.where(low_half, left, right))
        sums = jnp.concatenate(tiles, axis=1)
        sums = jnp.where(live, sums, 0.0).astype(jnp.bfloat16).astype(p_ref.dtype)
        s_ref[width * r : width * (r + 1), :] = sums
        return carry

    for r in range(rows):
        row(r, 0)
    owners = [jnp.bitwise_and(aggs_ref[0, step * rows + r], AGG_DEV - 1) for r in range(rows)]
    for a in range(AGG_DEV):
        spread = jnp.concatenate(
            [jnp.where(owners[r] == a, p_ref[r], jnp.zeros_like(p_ref[r])) for r in range(rows)], axis=0
        )
        o_ref[a] += lax.dot_general(spread, s_ref[...], (((0,), (0,)), ((), ())), preferred_element_type=jnp.float32)


def coarse_rows(fine, ghosts, own, cols, aggs, live_count, base, rows=8, group=2, transpose_lhs=True, interpret=False):
    capacity, width, span = fine.shape
    slot_width = 3 * AGG_DEV
    ghost_count = ghosts.shape[0]
    doubled = jnp.concatenate([ghosts, ghosts], axis=2)
    grid_spec = pltpu.PrefetchScalarGridSpec(
        num_scalar_prefetch=4,
        grid=(capacity // rows,),
        in_specs=[
            pl.BlockSpec((rows, width, span), lambda b, *_: (b, 0, 0)),
            pl.BlockSpec((ghost_count, width, 2 * width), lambda b, *_: (0, 0, 0)),
            pl.BlockSpec((rows, width, width), lambda b, *_: (b, 0, 0)),
        ],
        out_specs=pl.BlockSpec((AGG_DEV, width, slot_width * width), lambda b, *_: (0, 0, 0)),
        scratch_shapes=[
            pltpu.VMEM((slot_width, width, 2 * width), jnp.float32),
            pltpu.VMEM((slot_width, width, 2 * width), jnp.float32),
            pltpu.VMEM((rows * width, span), own.dtype),
        ],
    )
    kernel = functools.partial(coarse_kernel, group=group, transpose_lhs=transpose_lhs, capacity=capacity)
    return pl.pallas_call(
        kernel,
        grid_spec=grid_spec,
        out_shape=jax.ShapeDtypeStruct((AGG_DEV, width, slot_width * width), jnp.float32),
        compiler_params=pltpu.CompilerParams(dimension_semantics=("arbitrary",)),
        interpret=interpret,
    )(cols, aggs, live_count, base, fine, doubled, own)


def extended(block, sides, width):
    for axis, dim in sides:
        count = lax.axis_size(axis)
        forward = [(i, i + 1) for i in range(count - 1)]
        backward = [(target, source) for source, target in forward]
        low = lax.ppermute(
            lax.slice_in_dim(block, block.shape[dim] - width, None, axis=dim), axis, forward
        )
        high = lax.ppermute(lax.slice_in_dim(block, 0, width, axis=dim), axis, backward)
        block = jnp.concatenate([low, block, high], axis=dim)
    return block


def local(fine_matrix_blocks, prolongator, block_columns, block_aggregates, live_counts):
    capacity = fine_matrix_blocks.shape[0]
    position = lax.axis_index(("grp", "dom"))
    ghosts = extended(prolongator, ((("grp", "dom"), 0),), capacity)
    base = jnp.reshape((position - 1) * capacity, (1,)).astype(jnp.int32)
    coarse = coarse_rows(
        fine_matrix_blocks, ghosts, prolongator, block_columns.T, block_aggregates.T, live_counts, base
    )
    groups_count = lax.axis_size("grp")
    places = lax.axis_size("dom")
    step_stride = places // groups_count
    pairs = [
        (g * places + q, g * places + (q + step_stride * g) % places)
        for g in range(groups_count)
        for q in range(places)
    ]
    rotated = lax.ppermute(coarse.astype(jnp.bfloat16), ("grp", "dom"), pairs)
    copies = jnp.broadcast_to(rotated[None], (groups_count,) + rotated.shape)
    result = lax.all_to_all(copies, "grp", 0, 0, tiled=True).astype(jnp.float32)
    return result.reshape((groups_count * AGG_DEV,) + coarse.shape[1:])


def solution(mesh):
    return jax.shard_map(
        local,
        mesh=mesh,
        in_specs=(
            P(("grp", "dom"), None, None),
            P(("grp", "dom"), None, None),
            P(("grp", "dom"), None),
            P(("grp", "dom"), None),
            P(("grp", "dom")),
        ),
        out_specs=P("dom", None, None),
        check_vma=False,
    )
```

```python
import functools
import jax
import jax.numpy as jnp
from jax import lax
from jax.experimental import pallas as pl
from jax.experimental.pallas import tpu as pltpu
from jax.sharding import PartitionSpec as P

AGG_DEV = 4


def coarse_kernel(cols_ref, aggs_ref, live_ref, base_ref, f_ref, g_ref, p_ref, o_ref, even_ref, odd_ref, s_ref, acc_ref, *, group, transpose_lhs, capacity):
    step = pl.program_id(0)
    rows = f_ref.shape[0]
    width = p_ref.shape[1]
    blocks = f_ref.shape[2] // width
    slots = even_ref.shape[0]
    ghost_count = g_ref.shape[0]

    @pl.when(step == 0)
    def _():
        acc_ref[...] = jnp.zeros_like(acc_ref)

    lane = lax.broadcasted_iota(jnp.int32, (width, 2 * width), 1)
    low_half = lane < width
    base = base_ref[0]

    def place(r_i, k):
        c = jnp.clip(cols_ref[k, r_i] - base, 0, ghost_count - 1)
        t = AGG_DEV * (c // capacity) + jnp.bitwise_and(aggs_ref[k, r_i], AGG_DEV - 1)
        return c, t

    def row(r, carry):
        i = step * rows + r
        even_ref[...] = jnp.zeros_like(even_ref)
        odd_ref[...] = jnp.zeros_like(odd_ref)
        for j in range(blocks // group):
            ks = [group * j + m for m in range(group)]
            placed = [place(i, k) for k in ks]
            pieces = []
            for m, (c, _) in enumerate(placed):
                raw = g_ref[c]
                tile = jnp.concatenate([raw, raw], axis=1)
                pieces.append(jnp.where(low_half if m % 2 == 0 else ~low_half, tile, jnp.zeros_like(tile)))
            if group == 2:
                block = jnp.concatenate(pieces, axis=0)
            else:
                zero = jnp.zeros((2 * width, 2 * width), pieces[0].dtype)
                top = jnp.concatenate([jnp.concatenate(pieces[:2], axis=0), zero], axis=1)
                bottom = jnp.concatenate([zero, jnp.concatenate(pieces[2:], axis=0)], axis=1)
                block = jnp.concatenate([top, bottom], axis=0)
            part = jnp.dot(
                f_ref[r, :, group * width * j : group * width * (j + 1)], block, preferred_element_type=jnp.float32
            )
            for h in range(group // 2):
                half = part[:, 2 * width * h : 2 * width * (h + 1)]
                even_ref[placed[2 * h][1]] += half
                odd_ref[placed[2 * h + 1][1]] += half
        live = i < live_ref[0]
        tiles = []
        for u in range(slots // 2):
            left = even_ref[2 * u] + pltpu.roll(odd_ref[2 * u], width, 1)
            right = pltpu.roll(even_ref[2 * u + 1], width, 1) + odd_ref[2 * u + 1]
            tiles.append(jnp.where(low_half, left, right))
        sums = jnp.concatenate(tiles, axis=1)
        sums = jnp.where(live, sums, 0.0).astype(jnp.bfloat16).astype(p_ref.dtype)
        s_ref[width * r : width * (r + 1), :] = sums
        return carry

    for r in range(rows):
        row(r, 0)
    owners = [jnp.bitwise_and(aggs_ref[0, step * rows + r], AGG_DEV - 1) for r in range(rows)]
    for a in range(AGG_DEV):
        spread = jnp.concatenate(
            [jnp.where(owners[r] == a, p_ref[r], jnp.zeros_like(p_ref[r])) for r in range(rows)], axis=0
        )
        acc_ref[a] += lax.dot_general(spread, s_ref[...], (((0,), (0,)), ((), ())), preferred_element_type=jnp.float32)

    @pl.when(step == pl.num_programs(0) - 1)
    def _():
        o_ref[...] = acc_ref[...].astype(o_ref.dtype)


def coarse_rows(fine, ghosts, own, cols, aggs, live_count, base, rows=8, group=2, transpose_lhs=True, interpret=False):
    capacity, width, span = fine.shape
    slot_width = 3 * AGG_DEV
    ghost_count = ghosts.shape[0]
    grid_spec = pltpu.PrefetchScalarGridSpec(
        num_scalar_prefetch=4,
        grid=(capacity // rows,),
        in_specs=[
            pl.BlockSpec((rows, width, span), lambda b, *_: (b, 0, 0)),
            pl.BlockSpec(ghosts.shape, lambda b, *_: (0, 0, 0)),
            pl.BlockSpec((rows, width, width), lambda b, *_: (b, 0, 0)),
        ],
        out_specs=pl.BlockSpec((AGG_DEV, width, slot_width * width), lambda b, *_: (0, 0, 0)),
        scratch_shapes=[
            pltpu.VMEM((slot_width, width, 2 * width), jnp.float32),
            pltpu.VMEM((slot_width, width, 2 * width), jnp.float32),
            pltpu.VMEM((rows * width, span), own.dtype),
            pltpu.VMEM((AGG_DEV, width, slot_width * width), jnp.float32),
        ],
    )
    kernel = functools.partial(coarse_kernel, group=group, transpose_lhs=transpose_lhs, capacity=capacity)
    return pl.pallas_call(
        kernel,
        grid_spec=grid_spec,
        out_shape=jax.ShapeDtypeStruct((AGG_DEV, width, slot_width * width), jnp.bfloat16),
        compiler_params=pltpu.CompilerParams(dimension_semantics=("arbitrary",)),
        interpret=interpret,
    )(cols, aggs, live_count, base, fine, ghosts, own)


def extended(block, sides, width):
    for axis, dim in sides:
        count = lax.axis_size(axis)
        forward = [(i, i + 1) for i in range(count - 1)]
        backward = [(target, source) for source, target in forward]
        low = lax.ppermute(
            lax.slice_in_dim(block, block.shape[dim] - width, None, axis=dim), axis, forward
        )
        high = lax.ppermute(lax.slice_in_dim(block, 0, width, axis=dim), axis, backward)
        block = jnp.concatenate([low, block, high], axis=dim)
    return block


def local(fine_matrix_blocks, prolongator, block_columns, block_aggregates, live_counts):
    capacity = fine_matrix_blocks.shape[0]
    position = lax.axis_index(("grp", "dom"))
    ghosts = extended(prolongator, ((("grp", "dom"), 0),), capacity)
    base = jnp.reshape((position - 1) * capacity, (1,)).astype(jnp.int32)
    coarse = coarse_rows(
        fine_matrix_blocks, ghosts, prolongator, block_columns.T, block_aggregates.T, live_counts, base
    )
    groups_count = lax.axis_size("grp")
    places = lax.axis_size("dom")
    step_stride = places // groups_count
    pairs = [
        (g * places + q, g * places + (q + step_stride * g) % places)
        for g in range(groups_count)
        for q in range(places)
    ]
    rotated = lax.ppermute(coarse, ("grp", "dom"), pairs)
    copies = jnp.broadcast_to(rotated[None], (groups_count,) + rotated.shape)
    result = lax.all_to_all(copies, "grp", 0, 0, tiled=True).astype(jnp.float32)
    return result.reshape((groups_count * AGG_DEV,) + coarse.shape[1:])


def solution(mesh):
    return jax.shard_map(
        local,
        mesh=mesh,
        in_specs=(
            P(("grp", "dom"), None, None),
            P(("grp", "dom"), None, None),
            P(("grp", "dom"), None),
            P(("grp", "dom"), None),
            P(("grp", "dom")),
        ),
        out_specs=P("dom", None, None),
        check_vma=False,
    )
```

```python
import functools
import jax
import jax.numpy as jnp
from jax import lax
from jax.experimental import pallas as pl
from jax.experimental.pallas import tpu as pltpu
from jax.sharding import PartitionSpec as P

AGG_DEV = 4


def coarse_kernel(cols_ref, aggs_ref, live_ref, base_ref, f_ref, g_ref, p_ref, o_ref, tile_ref, s_ref, acc_ref, *, group, transpose_lhs, capacity):
    step = pl.program_id(0)
    rows = f_ref.shape[0]
    width = p_ref.shape[1]
    blocks = f_ref.shape[2] // width
    ghost_count = g_ref.shape[0]

    @pl.when(step == 0)
    def _():
        acc_ref[...] = jnp.zeros_like(acc_ref)

    lane = lax.broadcasted_iota(jnp.int32, (width, 2 * width), 1)
    low_half = lane < width
    base = base_ref[0]

    def place(r_i, k):
        c = jnp.clip(cols_ref[k, r_i] - base, 0, ghost_count - 1)
        t = AGG_DEV * (c // capacity) + jnp.bitwise_and(aggs_ref[k, r_i], AGG_DEV - 1)
        return c, t

    def row(r, carry):
        i = step * rows + r
        tile_ref[...] = jnp.zeros_like(tile_ref)
        for j in range(blocks // group):
            ks = [group * j + m for m in range(group)]
            placed = [place(i, k) for k in ks]
            pieces = []
            for m, (c, _) in enumerate(placed):
                raw = g_ref[c]
                tile = jnp.concatenate([raw, raw], axis=1)
                pieces.append(jnp.where(low_half if m % 2 == 0 else ~low_half, tile, jnp.zeros_like(tile)))
            if group == 2:
                block = jnp.concatenate(pieces, axis=0)
            else:
                zero = jnp.zeros((2 * width, 2 * width), pieces[0].dtype)
                top = jnp.concatenate([jnp.concatenate(pieces[:2], axis=0), zero], axis=1)
                bottom = jnp.concatenate([zero, jnp.concatenate(pieces[2:], axis=0)], axis=1)
                block = jnp.concatenate([top, bottom], axis=0)
            part = jnp.dot(
                f_ref[r, :, group * width * j : group * width * (j + 1)], block, preferred_element_type=jnp.float32
            )
            for h in range(group // 2):
                same = part[:, 2 * width * h : 2 * width * (h + 1)]
                swapped = pltpu.roll(same, width, 1)
                for m, first_src, second_src in ((0, same, swapped), (1, swapped, same)):
                    t = placed[2 * h + m][1]
                    odd = jnp.bitwise_and(t, 1) == 1
                    keep = jnp.logical_xor(low_half, odd)
                    tile_ref[t // 2] += jnp.where(keep, jnp.where(odd, second_src, first_src), 0.0)
        live = i < live_ref[0]
        sums = jnp.concatenate([tile_ref[u] for u in range(tile_ref.shape[0])], axis=1)
        sums = jnp.where(live, sums, 0.0).astype(jnp.bfloat16).astype(p_ref.dtype)
        s_ref[width * r : width * (r + 1), :] = sums
        return carry

    for r in range(rows):
        row(r, 0)
    owners = [jnp.bitwise_and(aggs_ref[0, step * rows + r], AGG_DEV - 1) for r in range(rows)]
    for a in range(AGG_DEV):
        spread = jnp.concatenate(
            [jnp.where(owners[r] == a, p_ref[r], jnp.zeros_like(p_ref[r])) for r in range(rows)], axis=0
        )
        acc_ref[a] += lax.dot_general(spread, s_ref[...], (((0,), (0,)), ((), ())), preferred_element_type=jnp.float32)

    @pl.when(step == pl.num_programs(0) - 1)
    def _():
        o_ref[...] = acc_ref[...].astype(o_ref.dtype)


def coarse_rows(fine, ghosts, own, cols, aggs, live_count, base, rows=8, group=2, transpose_lhs=True, interpret=False):
    capacity, width, span = fine.shape
    slot_width = 3 * AGG_DEV
    ghost_count = ghosts.shape[0]
    grid_spec = pltpu.PrefetchScalarGridSpec(
        num_scalar_prefetch=4,
        grid=(capacity // rows,),
        in_specs=[
            pl.BlockSpec((rows, width, span), lambda b, *_: (b, 0, 0)),
            pl.BlockSpec(ghosts.shape, lambda b, *_: (0, 0, 0)),
            pl.BlockSpec((rows, width, width), lambda b, *_: (b, 0, 0)),
        ],
        out_specs=pl.BlockSpec((AGG_DEV, width, slot_width * width), lambda b, *_: (0, 0, 0)),
        scratch_shapes=[
            pltpu.VMEM((slot_width // 2, width, 2 * width), jnp.float32),
            pltpu.VMEM((rows * width, span), own.dtype),
            pltpu.VMEM((AGG_DEV, width, slot_width * width), jnp.float32),
        ],
    )
    kernel = functools.partial(coarse_kernel, group=group, transpose_lhs=transpose_lhs, capacity=capacity)
    return pl.pallas_call(
        kernel,
        grid_spec=grid_spec,
        out_shape=jax.ShapeDtypeStruct((AGG_DEV, width, slot_width * width), jnp.bfloat16),
        compiler_params=pltpu.CompilerParams(dimension_semantics=("arbitrary",)),
        interpret=interpret,
    )(cols, aggs, live_count, base, fine, ghosts, own)


def extended(block, sides, width):
    for axis, dim in sides:
        count = lax.axis_size(axis)
        forward = [(i, i + 1) for i in range(count - 1)]
        backward = [(target, source) for source, target in forward]
        low = lax.ppermute(
            lax.slice_in_dim(block, block.shape[dim] - width, None, axis=dim), axis, forward
        )
        high = lax.ppermute(lax.slice_in_dim(block, 0, width, axis=dim), axis, backward)
        block = jnp.concatenate([low, block, high], axis=dim)
    return block


def local(fine_matrix_blocks, prolongator, block_columns, block_aggregates, live_counts):
    capacity = fine_matrix_blocks.shape[0]
    position = lax.axis_index(("grp", "dom"))
    ghosts = extended(prolongator, ((("grp", "dom"), 0),), capacity)
    base = jnp.reshape((position - 1) * capacity, (1,)).astype(jnp.int32)
    coarse = coarse_rows(
        fine_matrix_blocks, ghosts, prolongator, block_columns.T, block_aggregates.T, live_counts, base
    )
    groups_count = lax.axis_size("grp")
    places = lax.axis_size("dom")
    step_stride = places // groups_count
    pairs = [
        (g * places + q, g * places + (q + step_stride * g) % places)
        for g in range(groups_count)
        for q in range(places)
    ]
    rotated = lax.ppermute(coarse, ("grp", "dom"), pairs)
    copies = jnp.broadcast_to(rotated[None], (groups_count,) + rotated.shape)
    result = lax.all_to_all(copies, "grp", 0, 0, tiled=True).astype(jnp.float32)
    return result.reshape((groups_count * AGG_DEV,) + coarse.shape[1:])


def solution(mesh):
    return jax.shard_map(
        local,
        mesh=mesh,
        in_specs=(
            P(("grp", "dom"), None, None),
            P(("grp", "dom"), None, None),
            P(("grp", "dom"), None),
            P(("grp", "dom"), None),
            P(("grp", "dom")),
        ),
        out_specs=P("dom", None, None),
        check_vma=False,
    )
```

```python
import functools
import jax
import jax.numpy as jnp
from jax import lax
from jax.experimental import pallas as pl
from jax.experimental.pallas import tpu as pltpu
from jax.sharding import PartitionSpec as P

AGG_DEV = 4


def coarse_kernel(cols_ref, aggs_ref, live_ref, base_ref, f_ref, g_ref, p_ref, o_ref, tile_ref, s_ref, acc_ref, *, group, transpose_lhs, capacity):
    step = pl.program_id(0)
    rows = f_ref.shape[0]
    width = p_ref.shape[1]
    blocks = f_ref.shape[2] // width
    ghost_count = g_ref.shape[0]

    @pl.when(step == 0)
    def _():
        acc_ref[...] = jnp.zeros_like(acc_ref)

    lane = lax.broadcasted_iota(jnp.int32, (width, 2 * width), 1)
    low_half = lane < width
    base = base_ref[0]

    def place(r_i, k):
        c = jnp.clip(cols_ref[k, r_i] - base, 0, ghost_count - 1)
        t = AGG_DEV * (c // capacity) + jnp.bitwise_and(aggs_ref[k, r_i], AGG_DEV - 1)
        return c, t

    def row(r, carry):
        i = step * rows + r
        tile_ref[...] = jnp.zeros_like(tile_ref)
        for j in range(blocks // group):
            ks = [group * j + m for m in range(group)]
            placed = [place(i, k) for k in ks]
            pieces = []
            for m, (c, _) in enumerate(placed):
                tile = g_ref[c]
                pieces.append(jnp.where(low_half if m % 2 == 0 else ~low_half, tile, jnp.zeros_like(tile)))
            if group == 2:
                block = jnp.concatenate(pieces, axis=0)
            else:
                zero = jnp.zeros((2 * width, 2 * width), pieces[0].dtype)
                top = jnp.concatenate([jnp.concatenate(pieces[:2], axis=0), zero], axis=1)
                bottom = jnp.concatenate([zero, jnp.concatenate(pieces[2:], axis=0)], axis=1)
                block = jnp.concatenate([top, bottom], axis=0)
            part = jnp.dot(
                f_ref[r, :, group * width * j : group * width * (j + 1)], block, preferred_element_type=jnp.float32
            )
            for h in range(group // 2):
                same = part[:, 2 * width * h : 2 * width * (h + 1)]
                swapped = pltpu.roll(same, width, 1)
                for m, first_src, second_src in ((0, same, swapped), (1, swapped, same)):
                    t = placed[2 * h + m][1]
                    odd = jnp.bitwise_and(t, 1) == 1
                    keep = jnp.logical_xor(low_half, odd)
                    tile_ref[t // 2] += jnp.where(keep, jnp.where(odd, second_src, first_src), 0.0)
        live = i < live_ref[0]
        sums = jnp.concatenate([tile_ref[u] for u in range(tile_ref.shape[0])], axis=1)
        sums = jnp.where(live, sums, 0.0).astype(jnp.bfloat16).astype(p_ref.dtype)
        s_ref[width * r : width * (r + 1), :] = sums
        return carry

    for r in range(rows):
        row(r, 0)
    owners = [jnp.bitwise_and(aggs_ref[0, step * rows + r], AGG_DEV - 1) for r in range(rows)]
    for a in range(AGG_DEV):
        spread = jnp.concatenate(
            [jnp.where(owners[r] == a, p_ref[r], jnp.zeros_like(p_ref[r])) for r in range(rows)], axis=0
        )
        acc_ref[a] += lax.dot_general(spread, s_ref[...], (((0,), (0,)), ((), ())), preferred_element_type=jnp.float32)

    @pl.when(step == pl.num_programs(0) - 1)
    def _():
        o_ref[...] = acc_ref[...].astype(o_ref.dtype)


def coarse_rows(fine, ghosts, own, cols, aggs, live_count, base, rows=16, group=2, transpose_lhs=True, interpret=False):
    capacity, width, span = fine.shape
    slot_width = 3 * AGG_DEV
    ghost_count = ghosts.shape[0]
    doubled = jnp.concatenate([ghosts, ghosts], axis=2)
    grid_spec = pltpu.PrefetchScalarGridSpec(
        num_scalar_prefetch=4,
        grid=(capacity // rows,),
        in_specs=[
            pl.BlockSpec((rows, width, span), lambda b, *_: (b, 0, 0)),
            pl.BlockSpec(doubled.shape, lambda b, *_: (0, 0, 0)),
            pl.BlockSpec((rows, width, width), lambda b, *_: (b, 0, 0)),
        ],
        out_specs=pl.BlockSpec((AGG_DEV, width, slot_width * width), lambda b, *_: (0, 0, 0)),
        scratch_shapes=[
            pltpu.VMEM((slot_width // 2, width, 2 * width), jnp.float32),
            pltpu.VMEM((rows * width, span), own.dtype),
            pltpu.VMEM((AGG_DEV, width, slot_width * width), jnp.float32),
        ],
    )
    kernel = functools.partial(coarse_kernel, group=group, transpose_lhs=transpose_lhs, capacity=capacity)
    return pl.pallas_call(
        kernel,
        grid_spec=grid_spec,
        out_shape=jax.ShapeDtypeStruct((AGG_DEV, width, slot_width * width), jnp.bfloat16),
        compiler_params=pltpu.CompilerParams(dimension_semantics=("arbitrary",)),
        interpret=interpret,
    )(cols, aggs, live_count, base, fine, doubled, own)


def extended(block, sides, width):
    for axis, dim in sides:
        count = lax.axis_size(axis)
        forward = [(i, i + 1) for i in range(count - 1)]
        backward = [(target, source) for source, target in forward]
        low = lax.ppermute(
            lax.slice_in_dim(block, block.shape[dim] - width, None, axis=dim), axis, forward
        )
        high = lax.ppermute(lax.slice_in_dim(block, 0, width, axis=dim), axis, backward)
        block = jnp.concatenate([low, block, high], axis=dim)
    return block


def local(fine_matrix_blocks, prolongator, block_columns, block_aggregates, live_counts):
    capacity = fine_matrix_blocks.shape[0]
    position = lax.axis_index(("grp", "dom"))
    ghosts = extended(prolongator, ((("grp", "dom"), 0),), capacity)
    base = jnp.reshape((position - 1) * capacity, (1,)).astype(jnp.int32)
    coarse = coarse_rows(
        fine_matrix_blocks, ghosts, prolongator, block_columns.T, block_aggregates.T, live_counts, base
    )
    groups_count = lax.axis_size("grp")
    places = lax.axis_size("dom")
    step_stride = places // groups_count
    pairs = [
        (g * places + q, g * places + (q + step_stride * g) % places)
        for g in range(groups_count)
        for q in range(places)
    ]
    rotated = lax.ppermute(coarse, ("grp", "dom"), pairs)
    copies = jnp.broadcast_to(rotated[None], (groups_count,) + rotated.shape)
    result = lax.all_to_all(copies, "grp", 0, 0, tiled=True).astype(jnp.float32)
    return result.reshape((groups_count * AGG_DEV,) + coarse.shape[1:])


def solution(mesh):
    return jax.shard_map(
        local,
        mesh=mesh,
        in_specs=(
            P(("grp", "dom"), None, None),
            P(("grp", "dom"), None, None),
            P(("grp", "dom"), None),
            P(("grp", "dom"), None),
            P(("grp", "dom")),
        ),
        out_specs=P("dom", None, None),
        check_vma=False,
    )
```

```python
import functools
import jax
import jax.numpy as jnp
from jax import lax
from jax.experimental import pallas as pl
from jax.experimental.pallas import tpu as pltpu
from jax.sharding import PartitionSpec as P

AGG_DEV = 4


def coarse_kernel(cols_ref, aggs_ref, live_ref, base_ref, f_ref, g_ref, p_ref, o_ref, tile_ref, s_ref, acc_ref, *, group, transpose_lhs, capacity):
    step = pl.program_id(0)
    rows = f_ref.shape[0]
    width = p_ref.shape[1]
    blocks = f_ref.shape[2] // width
    ghost_count = g_ref.shape[0]

    @pl.when(step == 0)
    def _():
        acc_ref[...] = jnp.zeros_like(acc_ref)

    lane = lax.broadcasted_iota(jnp.int32, (width, 2 * width), 1)
    low_half = lane < width
    base = base_ref[0]

    def place(r_i, k):
        c = jnp.clip(cols_ref[k, r_i] - base, 0, ghost_count - 1)
        t = AGG_DEV * (c // capacity) + jnp.bitwise_and(aggs_ref[k, r_i], AGG_DEV - 1)
        return c, t

    def row(r, carry):
        i = step * rows + r
        tile_ref[...] = jnp.zeros_like(tile_ref)
        for j in range(blocks // group):
            ks = [group * j + m for m in range(group)]
            placed = [place(i, k) for k in ks]
            pieces = []
            for m, (c, _) in enumerate(placed):
                tile = g_ref[c]
                pieces.append(jnp.where(low_half if m % 2 == 0 else ~low_half, tile, jnp.zeros_like(tile)))
            if group == 2:
                block = jnp.concatenate(pieces, axis=0)
            else:
                zero = jnp.zeros((2 * width, 2 * width), pieces[0].dtype)
                top = jnp.concatenate([jnp.concatenate(pieces[:2], axis=0), zero], axis=1)
                bottom = jnp.concatenate([zero, jnp.concatenate(pieces[2:], axis=0)], axis=1)
                block = jnp.concatenate([top, bottom], axis=0)
            part = jnp.dot(
                f_ref[r, :, group * width * j : group * width * (j + 1)], block, preferred_element_type=jnp.float32
            )
            for h in range(group // 2):
                same = part[:, 2 * width * h : 2 * width * (h + 1)]
                swapped = pltpu.roll(same, width, 1)
                for m, first_src, second_src in ((0, same, swapped), (1, swapped, same)):
                    t = placed[2 * h + m][1]
                    odd = jnp.bitwise_and(t, 1) == 1
                    keep = jnp.logical_xor(low_half, odd)
                    tile_ref[t // 2] += jnp.where(keep, jnp.where(odd, second_src, first_src), 0.0)
        live = i < live_ref[0]
        sums = jnp.concatenate([tile_ref[u] for u in range(tile_ref.shape[0])], axis=1)
        sums = jnp.where(live, sums, 0.0).astype(jnp.bfloat16).astype(p_ref.dtype)
        s_ref[width * r : width * (r + 1), :] = sums
        return carry

    for r in range(rows):
        row(r, 0)
    owners = [jnp.bitwise_and(aggs_ref[0, step * rows + r], AGG_DEV - 1) for r in range(rows)]
    for a in range(AGG_DEV):
        spread = jnp.concatenate(
            [jnp.where(owners[r] == a, p_ref[r], jnp.zeros_like(p_ref[r])) for r in range(rows)], axis=0
        )
        acc_ref[a] += lax.dot_general(spread, s_ref[...], (((0,), (0,)), ((), ())), preferred_element_type=jnp.float32)

    @pl.when(step == pl.num_programs(0) - 1)
    def _():
        o_ref[...] = acc_ref[...].astype(o_ref.dtype)


def coarse_rows(fine, ghosts, own, cols, aggs, live_count, base, rows=8, group=2, transpose_lhs=True, interpret=False):
    capacity, width, span = fine.shape
    slot_width = 3 * AGG_DEV
    ghost_count = ghosts.shape[0]
    doubled = jnp.concatenate([ghosts, ghosts], axis=2)
    grid_spec = pltpu.PrefetchScalarGridSpec(
        num_scalar_prefetch=4,
        grid=(capacity // rows,),
        in_specs=[
            pl.BlockSpec((rows, width, span), lambda b, *_: (b, 0, 0)),
            pl.BlockSpec(doubled.shape, lambda b, *_: (0, 0, 0)),
            pl.BlockSpec((rows, width, width), lambda b, *_: (b, 0, 0)),
        ],
        out_specs=pl.BlockSpec((AGG_DEV, width, slot_width * width), lambda b, *_: (0, 0, 0)),
        scratch_shapes=[
            pltpu.VMEM((slot_width // 2, width, 2 * width), jnp.float32),
            pltpu.VMEM((rows * width, span), own.dtype),
            pltpu.VMEM((AGG_DEV, width, slot_width * width), jnp.float32),
        ],
    )
    kernel = functools.partial(coarse_kernel, group=group, transpose_lhs=transpose_lhs, capacity=capacity)
    return pl.pallas_call(
        kernel,
        grid_spec=grid_spec,
        out_shape=jax.ShapeDtypeStruct((AGG_DEV, width, slot_width * width), jnp.bfloat16),
        compiler_params=pltpu.CompilerParams(dimension_semantics=("arbitrary",)),
        interpret=interpret,
    )(cols, aggs, live_count, base, fine, doubled, own)


def extended(block, sides, width):
    for axis, dim in sides:
        count = lax.axis_size(axis)
        forward = [(i, i + 1) for i in range(count - 1)]
        backward = [(target, source) for source, target in forward]
        low = lax.ppermute(
            lax.slice_in_dim(block, block.shape[dim] - width, None, axis=dim), axis, forward
        )
        high = lax.ppermute(lax.slice_in_dim(block, 0, width, axis=dim), axis, backward)
        block = jnp.concatenate([low, block, high], axis=dim)
    return block


def local(fine_matrix_blocks, prolongator, block_columns, block_aggregates, live_counts):
    capacity = fine_matrix_blocks.shape[0]
    position = lax.axis_index(("grp", "dom"))
    ghosts = extended(prolongator, ((("grp", "dom"), 0),), capacity)
    base = jnp.reshape((position - 1) * capacity, (1,)).astype(jnp.int32)
    coarse = coarse_rows(
        fine_matrix_blocks, ghosts, prolongator, block_columns.T, block_aggregates.T, live_counts, base
    )
    groups_count = lax.axis_size("grp")
    places = lax.axis_size("dom")
    step_stride = places // groups_count
    pairs = [
        (g * places + q, g * places + (q + step_stride * g) % places)
        for g in range(groups_count)
        for q in range(places)
    ]
    rotated = lax.ppermute(coarse, ("grp", "dom"), pairs)
    copies = jnp.broadcast_to(rotated[None], (groups_count,) + rotated.shape)
    result = lax.all_to_all(copies, "grp", 0, 0, tiled=True).astype(jnp.float32)
    return result.reshape((groups_count * AGG_DEV,) + coarse.shape[1:])


def solution(mesh):
    return jax.shard_map(
        local,
        mesh=mesh,
        in_specs=(
            P(("grp", "dom"), None, None),
            P(("grp", "dom"), None, None),
            P(("grp", "dom"), None),
            P(("grp", "dom"), None),
            P(("grp", "dom")),
        ),
        out_specs=P("dom", None, None),
        check_vma=False,
    )
```

```python
import functools
import jax
import jax.numpy as jnp
from jax import lax
from jax.experimental import pallas as pl
from jax.experimental.pallas import tpu as pltpu
from jax.sharding import PartitionSpec as P

AGG_DEV = 4


def coarse_kernel(cols_ref, aggs_ref, live_ref, base_ref, f_ref, g_ref, p_ref, o_ref, tile_ref, s_ref, acc_ref, *, group, transpose_lhs, capacity):
    step = pl.program_id(0)
    rows = f_ref.shape[0]
    width = p_ref.shape[1]
    blocks = f_ref.shape[2] // width
    ghost_count = g_ref.shape[0]

    @pl.when(step == 0)
    def _():
        acc_ref[...] = jnp.zeros_like(acc_ref)

    lane = lax.broadcasted_iota(jnp.int32, (width, 2 * width), 1)
    low_half = lane < width
    base = base_ref[0]

    def place(r_i, k):
        c = jnp.clip(cols_ref[k, r_i] - base, 0, ghost_count - 1)
        t = AGG_DEV * (c // capacity) + jnp.bitwise_and(aggs_ref[k, r_i], AGG_DEV - 1)
        return c, t

    def row(r, carry):
        i = step * rows + r
        tile_ref[...] = jnp.zeros_like(tile_ref)
        for j in range(blocks // group):
            ks = [group * j + m for m in range(group)]
            placed = [place(i, k) for k in ks]
            pieces = []
            for m, (c, _) in enumerate(placed):
                raw = g_ref[c]
                tile = jnp.concatenate([raw, raw], axis=1)
                pieces.append(jnp.where(low_half if m % 2 == 0 else ~low_half, tile, jnp.zeros_like(tile)))
            if group == 2:
                block = jnp.concatenate(pieces, axis=0)
            else:
                zero = jnp.zeros((2 * width, 2 * width), pieces[0].dtype)
                top = jnp.concatenate([jnp.concatenate(pieces[:2], axis=0), zero], axis=1)
                bottom = jnp.concatenate([zero, jnp.concatenate(pieces[2:], axis=0)], axis=1)
                block = jnp.concatenate([top, bottom], axis=0)
            part = jnp.dot(
                f_ref[r, :, group * width * j : group * width * (j + 1)], block, preferred_element_type=jnp.float32
            )
            for h in range(group // 2):
                same = part[:, 2 * width * h : 2 * width * (h + 1)]
                for m in range(2):
                    t = placed[2 * h + m][1]
                    parity = jnp.bitwise_and(t, 1)
                    moved = pltpu.roll(same, width * jnp.bitwise_xor(parity, m), 1)
                    keep = jnp.logical_xor(low_half, parity == 1)
                    tile_ref[t // 2] += jnp.where(keep, moved, 0.0)
        live = i < live_ref[0]
        sums = jnp.concatenate([tile_ref[u] for u in range(tile_ref.shape[0])], axis=1)
        sums = jnp.where(live, sums, 0.0).astype(jnp.bfloat16).astype(p_ref.dtype)
        s_ref[width * r : width * (r + 1), :] = sums
        return carry

    for r in range(rows):
        row(r, 0)
    owners = [jnp.bitwise_and(aggs_ref[0, step * rows + r], AGG_DEV - 1) for r in range(rows)]
    for a in range(AGG_DEV):
        spread = jnp.concatenate(
            [jnp.where(owners[r] == a, p_ref[r], jnp.zeros_like(p_ref[r])) for r in range(rows)], axis=0
        )
        acc_ref[a] += lax.dot_general(spread, s_ref[...], (((0,), (0,)), ((), ())), preferred_element_type=jnp.float32)

    @pl.when(step == pl.num_programs(0) - 1)
    def _():
        o_ref[...] = acc_ref[...].astype(o_ref.dtype)


def coarse_rows(fine, ghosts, own, cols, aggs, live_count, base, rows=8, group=2, transpose_lhs=True, interpret=False):
    capacity, width, span = fine.shape
    slot_width = 3 * AGG_DEV
    ghost_count = ghosts.shape[0]
    grid_spec = pltpu.PrefetchScalarGridSpec(
        num_scalar_prefetch=4,
        grid=(capacity // rows,),
        in_specs=[
            pl.BlockSpec((rows, width, span), lambda b, *_: (b, 0, 0)),
            pl.BlockSpec(ghosts.shape, lambda b, *_: (0, 0, 0)),
            pl.BlockSpec((rows, width, width), lambda b, *_: (b, 0, 0)),
        ],
        out_specs=pl.BlockSpec((AGG_DEV, width, slot_width * width), lambda b, *_: (0, 0, 0)),
        scratch_shapes=[
            pltpu.VMEM((slot_width // 2, width, 2 * width), jnp.float32),
            pltpu.VMEM((rows * width, span), own.dtype),
            pltpu.VMEM((AGG_DEV, width, slot_width * width), jnp.float32),
        ],
    )
    kernel = functools.partial(coarse_kernel, group=group, transpose_lhs=transpose_lhs, capacity=capacity)
    return pl.pallas_call(
        kernel,
        grid_spec=grid_spec,
        out_shape=jax.ShapeDtypeStruct((AGG_DEV, width, slot_width * width), jnp.bfloat16),
        compiler_params=pltpu.CompilerParams(dimension_semantics=("arbitrary",)),
        interpret=interpret,
    )(cols, aggs, live_count, base, fine, ghosts, own)


def extended(block, sides, width):
    for axis, dim in sides:
        count = lax.axis_size(axis)
        forward = [(i, i + 1) for i in range(count - 1)]
        backward = [(target, source) for source, target in forward]
        low = lax.ppermute(
            lax.slice_in_dim(block, block.shape[dim] - width, None, axis=dim), axis, forward
        )
        high = lax.ppermute(lax.slice_in_dim(block, 0, width, axis=dim), axis, backward)
        block = jnp.concatenate([low, block, high], axis=dim)
    return block


def local(fine_matrix_blocks, prolongator, block_columns, block_aggregates, live_counts):
    capacity = fine_matrix_blocks.shape[0]
    position = lax.axis_index(("grp", "dom"))
    ghosts = extended(prolongator, ((("grp", "dom"), 0),), capacity)
    base = jnp.reshape((position - 1) * capacity, (1,)).astype(jnp.int32)
    coarse = coarse_rows(
        fine_matrix_blocks, ghosts, prolongator, block_columns.T, block_aggregates.T, live_counts, base
    )
    groups_count = lax.axis_size("grp")
    places = lax.axis_size("dom")
    step_stride = places // groups_count
    pairs = [
        (g * places + q, g * places + (q + step_stride * g) % places)
        for g in range(groups_count)
        for q in range(places)
    ]
    rotated = lax.ppermute(coarse, ("grp", "dom"), pairs)
    copies = jnp.broadcast_to(rotated[None], (groups_count,) + rotated.shape)
    result = lax.all_to_all(copies, "grp", 0, 0, tiled=True).astype(jnp.float32)
    return result.reshape((groups_count * AGG_DEV,) + coarse.shape[1:])


def solution(mesh):
    return jax.shard_map(
        local,
        mesh=mesh,
        in_specs=(
            P(("grp", "dom"), None, None),
            P(("grp", "dom"), None, None),
            P(("grp", "dom"), None),
            P(("grp", "dom"), None),
            P(("grp", "dom")),
        ),
        out_specs=P("dom", None, None),
        check_vma=False,
    )
```
